128 devices in a mesh: gop: 8 (over z, core), row: 16 (over x, y).
Axes of the slice: x: 4, y: 4, z: 4, core: 2. Of those that a mesh axis runs over, the one named last changes fastest.
Arguments:
- features: bfloat16 [8, 256, 480, 128], P('gop', 'row'), may hold values from -6 to 6
- filters: bfloat16 [3, 256, 2, 480, 128], P(None, None, None, 'row'), may hold values from -2.390625 to 2.390625
- anchors: int32 [8, 2], replicated, may hold values from 0 to 7, as said below
Outputs:
- joined: bfloat16 [8, 256, 480, 128], P('gop', 'row')
The draws below stay inside these ranges and needn't reach their ends.
Inputs may be any that keep to these rules, and one draw needn't show every extreme that they name: anchors[:, 0] lists each of the 8 frames exactly once; anchors[:, 1] takes exactly two distinct values, each in half of the rows.
All inputs are finite; a program needn't handle non-finite values.
Results may differ from the reference program's by a relative error of at most 0.0062.
Values may be sent and summed in bfloat16 or wider, within the bound.
No kernel may reach another device: no remote copies, remote signals or barrier semaphores. Data moves between devices by JAX's collectives and lax.ppermute only.
A program may use at most 256 MiB of HBM per device.

```python
import math
import jax
import jax.numpy as jnp
from jax import lax

C = 128
H = 256
W = 480
FRAMES = 8


def draw_anchors(key, part):
    key_first = jax.random.fold_in(key, 11)
    key_hubs = jax.random.fold_in(key, 12)
    key_sides = jax.random.fold_in(key, 13)
    first_col = jax.random.permutation(key_first, FRAMES).astype(jnp.int32)
    hub_frames = jax.random.permutation(key_hubs, FRAMES)[:2].astype(jnp.int32)
    sides = (jax.random.permutation(key_sides, FRAMES) < FRAMES // 2).astype(jnp.int32)
    second_col = hub_frames[sides]
    return jnp.stack([first_col, second_col], axis=1).astype(jnp.int32)


def levels(rng, dims, split, low, top_value):
    loudness, own = 1.0, jax.random.fold_in(rng, 6)
    for axis_at, shards_of in split:
        draws = jnp.exp(jax.random.uniform(jax.random.fold_in(own, axis_at), (shards_of,), jnp.float32, low / len(split), top_value / len(split)))
        loudness = loudness * jnp.repeat(draws, dims[axis_at] // shards_of).reshape([-1 if axis == axis_at else 1 for axis in range(len(dims))])
    return loudness


def gaussian(rng, shape, deviation, bound, shards=(), kind=jnp.bfloat16):
    drawn = deviation * jax.random.normal(rng, shape, jnp.float32)
    if shards:
        drawn = drawn * levels(rng, shape, shards, -0.22, 0.18)
    return jnp.clip(drawn, -bound, bound).astype(kind)


def setup_inputs(seed: int = 0) -> dict:
    splits = jax.random.split(jax.random.key(seed), 4)
    features = gaussian(splits[0], (FRAMES, H, W, C), 1.0, 6.0, ((0, 8), (1, 16)))
    filters = gaussian(splits[1], (3, H, 2, W, C), 0.4, 2.390625, ((3, 16),))
    anchors = draw_anchors(jax.random.fold_in(splits[3], 71), 0)
    return {"features": features, "filters": filters, "anchors": anchors}


def row_table(length):
    across = jnp.arange(length, dtype=jnp.int32)
    phases = across[:, None] * across[None, :] % length
    angles = phases.astype(jnp.float32) * (2.0 * math.pi / length)
    factor = 1.0 / math.sqrt(length)
    return jnp.concatenate([jnp.cos(angles) * factor, -jnp.sin(angles) * factor], axis=1).astype(jnp.bfloat16)

def column_matrix(length, sign):
    across = jnp.arange(length, dtype=jnp.int32)
    phases = across[:, None] * across[None, :] % length
    angles = phases.astype(jnp.float32) * (2.0 * math.pi / length)
    factor = 1.0 / math.sqrt(length)
    cosine = jnp.cos(angles) * factor
    sine_part = sign * jnp.sin(angles) * factor
    upper = jnp.stack([cosine, -sine_part], axis=-1)
    lower = jnp.stack([sine_part, cosine], axis=-1)
    return jnp.stack([upper, lower], axis=1).reshape(2 * length, 2 * length).astype(jnp.bfloat16)

def reference(features, filters, anchors):
    forward_rows = row_table(W)
    rows_wide = forward_rows.astype(jnp.float32)
    forward_cols = column_matrix(H, -1.0)
    inverse_cols = column_matrix(H, 1.0)
    filt_wide = filters.astype(jnp.float32)

    def spectrum(frame):
        rowwise = jnp.einsum('hwc,wk->hkc', frame.astype(jnp.float32), rows_wide).astype(jnp.bfloat16)
        stacked = rowwise.reshape(2 * H, W * C)
        result = jnp.dot(forward_cols, stacked, preferred_element_type=jnp.float32)
        return result.astype(jnp.bfloat16).reshape(H, 2, W, C)
    spectra = lax.map(spectrum, features)

    def output_frame(number):
        sources = (spectra[number], spectra[anchors[number, 0]], spectra[anchors[number, 1]])
        real_part = jnp.zeros((H, W, C), jnp.float32)
        imag_part = jnp.zeros((H, W, C), jnp.float32)
        for which_one in range(3):
            source_real = sources[which_one][:, 0].astype(jnp.float32)
            source_imag = sources[which_one][:, 1].astype(jnp.float32)
            gain_real = filt_wide[which_one, :, 0]
            gain_imag = filt_wide[which_one, :, 1]
            real_part = real_part + gain_real * source_real - gain_imag * source_imag
            imag_part = imag_part + gain_real * source_imag + gain_imag * source_real
        mixed = jnp.stack([real_part, imag_part], axis=1).astype(jnp.bfloat16)
        back = jnp.dot(inverse_cols, mixed.reshape(2 * H, W * C), preferred_element_type=jnp.float32)
        back = lax.optimization_barrier(back.astype(jnp.bfloat16))
        spatial = jnp.einsum('hkc,wk->hwc', back.reshape(H, 2 * W, C).astype(jnp.float32), rows_wide)
        return (features[number].astype(jnp.float32) + spatial).astype(jnp.bfloat16)
    return lax.map(output_frame, jnp.arange(FRAMES, dtype=jnp.int32))
```

```python
import math

import jax
import jax.numpy as jnp
from jax import lax
from jax.sharding import PartitionSpec as P


def row_table(length):
    across = jnp.arange(length, dtype=jnp.int32)
    phases = across[:, None] * across[None, :] % length
    angles = phases.astype(jnp.float32) * (2.0 * math.pi / length)
    factor = 1.0 / math.sqrt(length)
    return jnp.concatenate([jnp.cos(angles) * factor, -jnp.sin(angles) * factor], axis=1).astype(
        jnp.bfloat16
    )


def column_matrix(length, sign):
    across = jnp.arange(length, dtype=jnp.int32)
    phases = across[:, None] * across[None, :] % length
    angles = phases.astype(jnp.float32) * (2.0 * math.pi / length)
    factor = 1.0 / math.sqrt(length)
    cosine = jnp.cos(angles) * factor
    sine_part = sign * jnp.sin(angles) * factor
    upper = jnp.stack([cosine, -sine_part], axis=-1)
    lower = jnp.stack([sine_part, cosine], axis=-1)
    return jnp.stack([upper, lower], axis=1).reshape(2 * length, 2 * length).astype(jnp.bfloat16)


AXES = ("gop", "row")


def on_device(features, filters, anchors):
    frames = lax.psum(1, "gop")
    blocks = lax.psum(1, "row")
    _, hb, columns, chans = features.shape
    height = filters.shape[1]
    wb = columns // blocks
    cb = chans // frames
    me_gop = lax.axis_index("gop")

    forward_rows = row_table(columns)
    forward_cols = column_matrix(height, -1.0)
    forward_cols = forward_cols.reshape(height, 2, 2 * height).transpose(1, 0, 2).reshape(2 * height, 2 * height)
    inverse_cols = column_matrix(height, 1.0)
    inverse_cols = inverse_cols.reshape(2 * height, height, 2).transpose(0, 2, 1).reshape(2 * height, 2 * height)

    x = features[0]
    rowwise = jnp.einsum("hwc,wk->hkc", x, forward_rows, preferred_element_type=jnp.float32)
    rowwise = rowwise.astype(jnp.bfloat16)
    send = rowwise.reshape(hb, 2, blocks, wb, frames, cb).transpose(4, 2, 0, 1, 3, 5)
    send = send.reshape(frames * blocks, hb * 2, wb * cb)
    recv = lax.all_to_all(send, AXES, 0, 0, tiled=True)
    stacked = recv.reshape(frames, blocks * hb * 2, wb * cb)
    spectra = jnp.einsum("ab,fbn->fan", forward_cols, stacked, preferred_element_type=jnp.float32)
    spectra = spectra.astype(jnp.bfloat16).reshape(frames, 2, height, wb * cb)

    gains = filters.reshape(3, height, 2, wb, frames, cb)
    gains = lax.dynamic_index_in_dim(gains, me_gop, axis=4, keepdims=False)
    gains = gains.transpose(0, 2, 1, 3, 4).reshape(3, 2, height, wb * cb).astype(jnp.float32)

    first = jnp.take(spectra, anchors[:, 0], axis=0, mode="clip")
    second = jnp.take(spectra, anchors[:, 1], axis=0, mode="clip")
    sources = (spectra, first, second)
    real_part = jnp.zeros((frames, height, wb * cb), jnp.float32)
    imag_part = jnp.zeros((frames, height, wb * cb), jnp.float32)
    for which_one in range(3):
        source_real = sources[which_one][:, 0].astype(jnp.float32)
        source_imag = sources[which_one][:, 1].astype(jnp.float32)
        gain_real = gains[which_one, 0]
        gain_imag = gains[which_one, 1]
        real_part = real_part + gain_real * source_real - gain_imag * source_imag
        imag_part = imag_part + gain_real * source_imag + gain_imag * source_real
    mixed = jnp.stack([real_part, imag_part], axis=1).astype(jnp.bfloat16)
    mixed = mixed.reshape(frames, 2 * height, wb * cb)
    back = jnp.einsum("ab,fbn->fan", inverse_cols, mixed, preferred_element_type=jnp.float32)
    back = back.astype(jnp.bfloat16)
    send2 = back.reshape(frames * blocks, hb * 2, wb * cb)
    recv2 = lax.all_to_all(send2, AXES, 0, 0, tiled=True)
    recv2 = recv2.reshape(frames, blocks, hb, 2, wb, cb)
    table = forward_rows.reshape(columns, 2, blocks, wb)
    spatial = jnp.einsum("grhpkc,wprk->hwgc", recv2, table, preferred_element_type=jnp.float32)
    spatial = spatial.reshape(hb, columns, chans)
    out = (x.astype(jnp.float32) + spatial).astype(jnp.bfloat16)
    return out[None]


def solution(mesh):
    in_specs = (P("gop", "row", None, None), P(None, None, None, "row", None), P())
    out_specs = P("gop", "row", None, None)
    return jax.shard_map(
        on_device, mesh=mesh, in_specs=in_specs, out_specs=out_specs, check_vma=False
    )
```

```python
import math

import jax
import jax.numpy as jnp
from jax import lax
from jax.sharding import PartitionSpec as P


def row_table(length):
    across = jnp.arange(length, dtype=jnp.int32)
    phases = across[:, None] * across[None, :] % length
    angles = phases.astype(jnp.float32) * (2.0 * math.pi / length)
    factor = 1.0 / math.sqrt(length)
    return jnp.concatenate([jnp.cos(angles) * factor, -jnp.sin(angles) * factor], axis=1).astype(
        jnp.bfloat16
    )


def column_matrix(length, sign):
    rows = lax.broadcasted_iota(jnp.int32, (2 * length, 2 * length), 0)
    cols = lax.broadcasted_iota(jnp.int32, (2 * length, 2 * length), 1)
    k, p = rows // 2, rows % 2
    h, q = cols // 2, cols % 2
    phases = k * h % length
    angles = phases.astype(jnp.float32) * (2.0 * math.pi / length)
    factor = 1.0 / math.sqrt(length)
    cosine = jnp.cos(angles) * factor
    sine_part = sign * jnp.sin(angles) * factor
    value = jnp.where(p == q, cosine, jnp.where(p == 0, -sine_part, sine_part))
    return value.astype(jnp.bfloat16)


def on_device(features, filters, anchors):
    frames = lax.psum(1, "gop")
    blocks = lax.psum(1, "row")
    _, hb, columns, chans = features.shape
    height = filters.shape[1]
    wb = columns // blocks
    kb = height // frames
    me_gop = lax.axis_index("gop")

    forward_rows = row_table(columns)
    split_table = forward_rows.reshape(columns, 2, columns)
    forward_cols = column_matrix(height, -1.0)
    inverse_cols = column_matrix(height, 1.0)

    x = features[0]
    rowwise = jnp.einsum("hwc,wk->hkc", x, forward_rows, preferred_element_type=jnp.float32)
    rowwise = rowwise.astype(jnp.bfloat16).reshape(hb, 2, columns, chans)
    slab = lax.all_to_all(rowwise, "row", 2, 0, tiled=True)
    spectra = jnp.dot(
        forward_cols, slab.reshape(2 * height, wb * chans), preferred_element_type=jnp.float32
    ).astype(jnp.bfloat16)
    spectra = spectra.reshape(frames, kb, 2, wb, chans)
    every = lax.all_to_all(spectra, "gop", 0, 0, tiled=True)

    gains = lax.dynamic_slice_in_dim(filters, me_gop * kb, kb, axis=1).astype(jnp.float32)
    first = jnp.take(every, anchors[:, 0], axis=0, mode="clip")
    second = jnp.take(every, anchors[:, 1], axis=0, mode="clip")
    sources = (every, first, second)
    real_part = jnp.zeros((frames, kb, wb, chans), jnp.float32)
    imag_part = jnp.zeros((frames, kb, wb, chans), jnp.float32)
    for which_one in range(3):
        source_real = sources[which_one][:, :, 0].astype(jnp.float32)
        source_imag = sources[which_one][:, :, 1].astype(jnp.float32)
        gain_real = gains[which_one, :, 0]
        gain_imag = gains[which_one, :, 1]
        real_part = real_part + gain_real * source_real - gain_imag * source_imag
        imag_part = imag_part + gain_real * source_imag + gain_imag * source_real
    mixed = jnp.stack([real_part, imag_part], axis=2).astype(jnp.bfloat16)
    mine = lax.all_to_all(mixed, "gop", 0, 0, tiled=True)
    back = jnp.dot(
        inverse_cols, mine.reshape(2 * height, wb * chans), preferred_element_type=jnp.float32
    ).astype(jnp.bfloat16)
    back = back.reshape(height, 2, wb, chans)
    rows_back = lax.all_to_all(back, "row", 0, 2, tiled=True)
    spatial = jnp.einsum(
        "hpkc,wpk->hwc", rows_back, split_table, preferred_element_type=jnp.float32
    )
    out = (x.astype(jnp.float32) + spatial).astype(jnp.bfloat16)
    return out[None]


def solution(mesh):
    in_specs = (P("gop", "row", None, None), P(None, None, None, "row", None), P())
    out_specs = P("gop", "row", None, None)
    return jax.shard_map(
        on_device, mesh=mesh, in_specs=in_specs, out_specs=out_specs, check_vma=False
    )
```

```python
import math

import jax
import jax.numpy as jnp
from jax import lax
from jax.sharding import PartitionSpec as P


def row_table(length):
    across = jnp.arange(length, dtype=jnp.int32)
    phases = across[:, None] * across[None, :] % length
    angles = phases.astype(jnp.float32) * (2.0 * math.pi / length)
    factor = 1.0 / math.sqrt(length)
    return jnp.concatenate([jnp.cos(angles) * factor, -jnp.sin(angles) * factor], axis=1).astype(
        jnp.bfloat16
    )


def column_matrix(length, sign, row_of, col_of):
    rows = lax.broadcasted_iota(jnp.int32, (2 * length, 2 * length), 0)
    cols = lax.broadcasted_iota(jnp.int32, (2 * length, 2 * length), 1)
    k, p = row_of(rows)
    h, q = col_of(cols)
    phases = k * h % length
    angles = phases.astype(jnp.float32) * (2.0 * math.pi / length)
    factor = 1.0 / math.sqrt(length)
    cosine = jnp.cos(angles) * factor
    sine_part = sign * jnp.sin(angles) * factor
    value = jnp.where(p == q, cosine, jnp.where(p == 0, -sine_part, sine_part))
    return value.astype(jnp.bfloat16)


def interleaved(index):
    return index // 2, index % 2


def blocked(kb):
    def split(index):
        blk, rest = index // (2 * kb), index % (2 * kb)
        return blk * kb + rest % kb, rest // kb

    return split


def on_device(features, filters, anchors):
    frames = lax.psum(1, "gop")
    blocks = lax.psum(1, "row")
    _, hb, columns, chans = features.shape
    height = filters.shape[1]
    wb = columns // blocks
    kb = height // frames
    lanes = wb * chans
    me_gop = lax.axis_index("gop")

    forward_rows = row_table(columns)
    forward_cols = column_matrix(height, -1.0, blocked(kb), interleaved)
    inverse_cols = column_matrix(height, 1.0, interleaved, blocked(kb))

    x = features[0]
    rowwise = jnp.einsum("hwc,wk->hkc", x, forward_rows, preferred_element_type=jnp.float32)
    rowwise = rowwise.astype(jnp.bfloat16).reshape(hb, 2, columns, chans)
    slab = lax.all_to_all(rowwise, "row", 2, 0, tiled=True)
    spectra = jnp.dot(
        forward_cols, slab.reshape(2 * height, lanes), preferred_element_type=jnp.float32
    ).astype(jnp.bfloat16)
    spectra = spectra.reshape(frames, 2 * kb, lanes)
    every = lax.all_to_all(spectra, "gop", 0, 0, tiled=True)
    every = every.reshape(frames, 2, kb, lanes)

    gains = lax.dynamic_slice_in_dim(filters, me_gop * kb, kb, axis=1)
    gains = gains.transpose(0, 2, 1, 3, 4).reshape(3, 2, kb, lanes).astype(jnp.float32)
    outs = []
    for frame in range(frames):
        sources = (
            every[frame],
            lax.dynamic_index_in_dim(every, anchors[frame, 0], 0, keepdims=False),
            lax.dynamic_index_in_dim(every, anchors[frame, 1], 0, keepdims=False),
        )
        real_part = jnp.zeros((kb, lanes), jnp.float32)
        imag_part = jnp.zeros((kb, lanes), jnp.float32)
        for which_one in range(3):
            source_real = sources[which_one][0].astype(jnp.float32)
            source_imag = sources[which_one][1].astype(jnp.float32)
            gain_real = gains[which_one, 0]
            gain_imag = gains[which_one, 1]
            real_part = real_part + gain_real * source_real - gain_imag * source_imag
            imag_part = imag_part + gain_real * source_imag + gain_imag * source_real
        outs.append(jnp.stack([real_part, imag_part]))
    mixed = jnp.stack(outs).astype(jnp.bfloat16).reshape(frames, 2 * kb, lanes)
    mine = lax.all_to_all(mixed, "gop", 0, 0, tiled=True)
    back = jnp.dot(
        inverse_cols, mine.reshape(2 * height, lanes), preferred_element_type=jnp.float32
    ).astype(jnp.bfloat16)
    back = back.reshape(blocks, 2 * hb, lanes)
    rows_back = lax.all_to_all(back, "row", 0, 0, tiled=True)
    rows_back = rows_back.reshape(blocks, hb, 2, wb, chans)
    table = forward_rows.reshape(columns, 2, blocks, wb)
    spatial = jnp.einsum(
        "rhpkc,wprk->hwc", rows_back, table, preferred_element_type=jnp.float32
    )
    out = (x.astype(jnp.float32) + spatial).astype(jnp.bfloat16)
    return out[None]


def solution(mesh):
    in_specs = (P("gop", "row", None, None), P(None, None, None, "row", None), P())
    out_specs = P("gop", "row", None, None)
    return jax.shard_map(
        on_device, mesh=mesh, in_specs=in_specs, out_specs=out_specs, check_vma=False
    )
```

```python
import math

import jax
import jax.numpy as jnp
from jax import lax
from jax.sharding import PartitionSpec as P


def row_table(length):
    across = jnp.arange(length, dtype=jnp.int32)
    phases = across[:, None] * across[None, :] % length
    angles = phases.astype(jnp.float32) * (2.0 * math.pi / length)
    factor = 1.0 / math.sqrt(length)
    return jnp.concatenate([jnp.cos(angles) * factor, -jnp.sin(angles) * factor], axis=1).astype(
        jnp.bfloat16
    )


def column_matrix(length, sign, row_of, col_of):
    rows = lax.broadcasted_iota(jnp.int32, (2 * length, 2 * length), 0)
    cols = lax.broadcasted_iota(jnp.int32, (2 * length, 2 * length), 1)
    k, p = row_of(rows)
    h, q = col_of(cols)
    phases = k * h % length
    angles = phases.astype(jnp.float32) * (2.0 * math.pi / length)
    factor = 1.0 / math.sqrt(length)
    cosine = jnp.cos(angles) * factor
    sine_part = sign * jnp.sin(angles) * factor
    value = jnp.where(p == q, cosine, jnp.where(p == 0, -sine_part, sine_part))
    return value.astype(jnp.bfloat16)


def interleaved(index):
    return index // 2, index % 2


def blocked(kb):
    def split(index):
        blk, rest = index // (2 * kb), index % (2 * kb)
        return blk * kb + rest % kb, rest // kb

    return split


CHUNKS = 2


def on_device(features, filters, anchors):
    frames = lax.psum(1, "gop")
    blocks = lax.psum(1, "row")
    _, hb, columns, chans = features.shape
    height = filters.shape[1]
    wb = columns // blocks
    kb = height // frames
    part = wb // CHUNKS
    lanes = part * chans
    me_gop = lax.axis_index("gop")

    table = row_table(columns).reshape(columns, 2, blocks, wb)
    forward_cols = column_matrix(height, -1.0, blocked(kb), interleaved)
    inverse_cols = column_matrix(height, 1.0, interleaved, blocked(kb))

    x = features[0]
    gains = lax.dynamic_slice_in_dim(filters, me_gop * kb, kb, axis=1)
    gains = gains.transpose(0, 2, 1, 3, 4)
    total = x.astype(jnp.float32)
    for chunk in range(CHUNKS):
        cols = slice(chunk * part, (chunk + 1) * part)
        piece = table[:, :, :, cols]
        rowwise = jnp.einsum("hwc,wprk->rhpkc", x, piece, preferred_element_type=jnp.float32)
        rowwise = rowwise.astype(jnp.bfloat16)
        slab = lax.all_to_all(rowwise, "row", 0, 0, tiled=True)
        spectra = jnp.dot(
            forward_cols, slab.reshape(2 * height, lanes), preferred_element_type=jnp.float32
        ).astype(jnp.bfloat16)
        spectra = spectra.reshape(frames, 2 * kb, lanes)
        every = lax.all_to_all(spectra, "gop", 0, 0, tiled=True)
        every = every.reshape(frames, 2, kb, lanes)
        gain = gains[:, :, :, cols].reshape(3, 2, kb, lanes).astype(jnp.float32)
        outs = []
        for frame in range(frames):
            sources = (
                every[frame],
                lax.dynamic_index_in_dim(every, anchors[frame, 0], 0, keepdims=False),
                lax.dynamic_index_in_dim(every, anchors[frame, 1], 0, keepdims=False),
            )
            real_part = jnp.zeros((kb, lanes), jnp.float32)
            imag_part = jnp.zeros((kb, lanes), jnp.float32)
            for which_one in range(3):
                source_real = sources[which_one][0].astype(jnp.float32)
                source_imag = sources[which_one][1].astype(jnp.float32)
                gain_real = gain[which_one, 0]
                gain_imag = gain[which_one, 1]
                real_part = real_part + gain_real * source_real - gain_imag * source_imag
                imag_part = imag_part + gain_real * source_imag + gain_imag * source_real
            outs.append(jnp.stack([real_part, imag_part]))
        mixed = jnp.stack(outs).astype(jnp.bfloat16).reshape(frames, 2 * kb, lanes)
        mine = lax.all_to_all(mixed, "gop", 0, 0, tiled=True)
        back = jnp.dot(
            inverse_cols, mine.reshape(2 * height, lanes), preferred_element_type=jnp.float32
        ).astype(jnp.bfloat16)
        back = back.reshape(blocks, 2 * hb, lanes)
        rows_back = lax.all_to_all(back, "row", 0, 0, tiled=True)
        rows_back = rows_back.reshape(blocks, hb, 2, part, chans)
        total = total + jnp.einsum(
            "rhpkc,wprk->hwc", rows_back, piece, preferred_element_type=jnp.float32
        )
    return total.astype(jnp.bfloat16)[None]


def solution(mesh):
    in_specs = (P("gop", "row", None, None), P(None, None, None, "row", None), P())
    out_specs = P("gop", "row", None, None)
    return jax.shard_map(
        on_device, mesh=mesh, in_specs=in_specs, out_specs=out_specs, check_vma=False
    )
```

```python
import math

import jax
import jax.numpy as jnp
from jax import lax
from jax.sharding import PartitionSpec as P


def row_table(length):
    across = jnp.arange(length, dtype=jnp.int32)
    phases = across[:, None] * across[None, :] % length
    angles = phases.astype(jnp.float32) * (2.0 * math.pi / length)
    factor = 1.0 / math.sqrt(length)
    return jnp.concatenate([jnp.cos(angles) * factor, -jnp.sin(angles) * factor], axis=1).astype(
        jnp.bfloat16
    )


def column_matrix(length, sign, row_of, col_of):
    rows = lax.broadcasted_iota(jnp.int32, (2 * length, 2 * length), 0)
    cols = lax.broadcasted_iota(jnp.int32, (2 * length, 2 * length), 1)
    k, p = row_of(rows)
    h, q = col_of(cols)
    phases = k * h % length
    angles = phases.astype(jnp.float32) * (2.0 * math.pi / length)
    factor = 1.0 / math.sqrt(length)
    cosine = jnp.cos(angles) * factor
    sine_part = sign * jnp.sin(angles) * factor
    value = jnp.where(p == q, cosine, jnp.where(p == 0, -sine_part, sine_part))
    return value.astype(jnp.bfloat16)


def interleaved(index):
    return index // 2, index % 2


def blocked(kb):
    def split(index):
        blk, rest = index // (2 * kb), index % (2 * kb)
        return blk * kb + rest % kb, rest // kb

    return split


CHUNKS = 2


def shifted(kb, frames, me, sign):
    def split(index):
        s, rest = index // (2 * kb), index % (2 * kb)
        return ((me + sign * s) % frames) * kb + rest % kb, rest // kb

    return split


def on_device(features, filters, anchors):
    frames = lax.psum(1, "gop")
    blocks = lax.psum(1, "row")
    _, hb, columns, chans = features.shape
    height = filters.shape[1]
    wb = columns // blocks
    kb = height // frames
    part = wb // CHUNKS
    lanes = part * chans
    me = lax.axis_index("gop")

    table = row_table(columns).reshape(columns, 2, blocks, wb)
    forward_cols = column_matrix(height, -1.0, shifted(kb, frames, me, 1), interleaved)
    inverse_cols = column_matrix(height, 1.0, interleaved, shifted(kb, frames, me, -1))
    shifts = [[(i, (i + s) % frames) for i in range(frames)] for s in range(frames)]

    x = features[0]
    gains = lax.dynamic_slice_in_dim(filters, me * kb, kb, axis=1)
    gains = gains.transpose(0, 2, 1, 3, 4)
    total = x.astype(jnp.float32)
    for chunk in range(CHUNKS):
        cols = slice(chunk * part, (chunk + 1) * part)
        piece = table[:, :, :, cols]
        rowwise = jnp.einsum("hwc,wprk->rhpkc", x, piece, preferred_element_type=jnp.float32)
        rowwise = rowwise.astype(jnp.bfloat16)
        slab = lax.all_to_all(rowwise, "row", 0, 0, tiled=True)
        spectra = jnp.dot(
            forward_cols, slab.reshape(2 * height, lanes), preferred_element_type=jnp.float32
        ).astype(jnp.bfloat16)
        spectra = spectra.reshape(frames, 2, kb, lanes)
        received = [spectra[0]] + [
            lax.ppermute(spectra[s], "gop", shifts[s]) for s in range(1, frames)
        ]
        every = jnp.stack(received)
        gain = gains[:, :, :, cols].reshape(3, 2, kb, lanes).astype(jnp.float32)
        outs = []
        for s in range(frames):
            frame = (me + s) % frames
            picks = (
                (me - frame) % frames,
                (me - anchors[frame, 0]) % frames,
                (me - anchors[frame, 1]) % frames,
            )
            sources = [lax.dynamic_index_in_dim(every, pick, 0, keepdims=False) for pick in picks]
            real_part = jnp.zeros((kb, lanes), jnp.float32)
            imag_part = jnp.zeros((kb, lanes), jnp.float32)
            for which_one in range(3):
                source_real = sources[which_one][0].astype(jnp.float32)
                source_imag = sources[which_one][1].astype(jnp.float32)
                gain_real = gain[which_one, 0]
                gain_imag = gain[which_one, 1]
                real_part = real_part + gain_real * source_real - gain_imag * source_imag
                imag_part = imag_part + gain_real * source_imag + gain_imag * source_real
            outs.append(jnp.stack([real_part, imag_part]).astype(jnp.bfloat16))
        mine = [outs[0]] + [lax.ppermute(outs[s], "gop", shifts[s]) for s in range(1, frames)]
        mine = jnp.stack(mine)
        back = jnp.dot(
            inverse_cols, mine.reshape(2 * height, lanes), preferred_element_type=jnp.float32
        ).astype(jnp.bfloat16)
        back = back.reshape(blocks, 2 * hb, lanes)
        rows_back = lax.all_to_all(back, "row", 0, 0, tiled=True)
        rows_back = rows_back.reshape(blocks, hb, 2, part, chans)
        total = total + jnp.einsum(
            "rhpkc,wprk->hwc", rows_back, piece, preferred_element_type=jnp.float32
        )
    return total.astype(jnp.bfloat16)[None]


def solution(mesh):
    in_specs = (P("gop", "row", None, None), P(None, None, None, "row", None), P())
    out_specs = P("gop", "row", None, None)
    return jax.shard_map(
        on_device, mesh=mesh, in_specs=in_specs, out_specs=out_specs, check_vma=False
    )
```

```python
import math

import jax
import jax.numpy as jnp
from jax import lax
from jax.sharding import PartitionSpec as P


def row_table(length):
    across = jnp.arange(length, dtype=jnp.int32)
    phases = across[:, None] * across[None, :] % length
    angles = phases.astype(jnp.float32) * (2.0 * math.pi / length)
    factor = 1.0 / math.sqrt(length)
    return jnp.concatenate([jnp.cos(angles) * factor, -jnp.sin(angles) * factor], axis=1).astype(
        jnp.bfloat16
    )


def column_matrix(length, sign, row_of, col_of):
    rows = lax.broadcasted_iota(jnp.int32, (2 * length, 2 * length), 0)
    cols = lax.broadcasted_iota(jnp.int32, (2 * length, 2 * length), 1)
    k, p = row_of(rows)
    h, q = col_of(cols)
    phases = k * h % length
    angles = phases.astype(jnp.float32) * (2.0 * math.pi / length)
    factor = 1.0 / math.sqrt(length)
    cosine = jnp.cos(angles) * factor
    sine_part = sign * jnp.sin(angles) * factor
    value = jnp.where(p == q, cosine, jnp.where(p == 0, -sine_part, sine_part))
    return value.astype(jnp.bfloat16)


def interleaved(index):
    return index // 2, index % 2


def blocked(kb):
    def split(index):
        blk, rest = index // (2 * kb), index % (2 * kb)
        return blk * kb + rest % kb, rest // kb

    return split


CHUNKS = 2


def shifted(kb, frames, me, sign):
    def split(index):
        s, rest = index // (2 * kb), index % (2 * kb)
        return ((me + sign * s) % frames) * kb + rest % kb, rest // kb

    return split


def on_device(features, filters, anchors):
    frames = lax.psum(1, "gop")
    blocks = lax.psum(1, "row")
    _, hb, columns, chans = features.shape
    height = filters.shape[1]
    wb = columns // blocks
    kb = height // frames
    part = wb // CHUNKS
    lanes = part * chans
    me = lax.axis_index("gop")

    table = row_table(columns).reshape(columns, 2, blocks, wb)
    forward_cols = column_matrix(height, -1.0, shifted(kb, frames, me, 1), interleaved)
    inverse_cols = column_matrix(height, 1.0, interleaved, shifted(kb, frames, me, -1))
    shifts = [[(i, (i + s) % frames) for i in range(frames)] for s in range(frames)]

    x = features[0]
    gains = lax.dynamic_slice_in_dim(filters, me * kb, kb, axis=1)
    gains = gains.transpose(0, 2, 1, 3, 4)
    def mix(every, gain):
        outs = []
        for s in range(frames):
            frame = (me + s) % frames
            picks = (
                (me - frame) % frames,
                (me - anchors[frame, 0]) % frames,
                (me - anchors[frame, 1]) % frames,
            )
            sources = [lax.dynamic_index_in_dim(every, pick, 0, keepdims=False) for pick in picks]
            real_part = jnp.zeros((kb, lanes), jnp.float32)
            imag_part = jnp.zeros((kb, lanes), jnp.float32)
            for which_one in range(3):
                source_real = sources[which_one][0].astype(jnp.float32)
                source_imag = sources[which_one][1].astype(jnp.float32)
                gain_real = gain[which_one, 0]
                gain_imag = gain[which_one, 1]
                real_part = real_part + gain_real * source_real - gain_imag * source_imag
                imag_part = imag_part + gain_real * source_imag + gain_imag * source_real
            outs.append(jnp.stack([real_part, imag_part]).astype(jnp.bfloat16))
        return outs

    def exchange(pieces):
        return [pieces[0]] + [lax.ppermute(pieces[s], "gop", shifts[s]) for s in range(1, frames)]

    chunks = [slice(c * part, (c + 1) * part) for c in range(CHUNKS)]
    pieces = [table[:, :, :, cols] for cols in chunks]
    slabs = []
    for chunk in range(CHUNKS):
        rowwise = jnp.einsum(
            "hwc,wprk->rhpkc", x, pieces[chunk], preferred_element_type=jnp.float32
        ).astype(jnp.bfloat16)
        slabs.append(lax.all_to_all(rowwise, "row", 0, 0, tiled=True))
    everys = []
    for chunk in range(CHUNKS):
        spectra = jnp.dot(
            forward_cols, slabs[chunk].reshape(2 * height, lanes), preferred_element_type=jnp.float32
        ).astype(jnp.bfloat16)
        spectra = spectra.reshape(frames, 2, kb, lanes)
        if chunk:
            spectra, _ = lax.optimization_barrier((spectra, everys[-1]))
        everys.append(jnp.stack(exchange([spectra[s] for s in range(frames)])))
    mines = []
    for chunk in range(CHUNKS):
        gain = gains[:, :, :, chunks[chunk]].reshape(3, 2, kb, lanes).astype(jnp.float32)
        outs = mix(everys[chunk], gain)
        if chunk:
            outs, _ = lax.optimization_barrier((outs, mines[-1]))
        mines.append(jnp.stack(exchange(outs)))
    total = x.astype(jnp.float32)
    for chunk in range(CHUNKS):
        back = jnp.dot(
            inverse_cols, mines[chunk].reshape(2 * height, lanes), preferred_element_type=jnp.float32
        ).astype(jnp.bfloat16)
        back = back.reshape(blocks, 2 * hb, lanes)
        rows_back = lax.all_to_all(back, "row", 0, 0, tiled=True)
        rows_back = rows_back.reshape(blocks, hb, 2, part, chans)
        total = total + jnp.einsum(
            "rhpkc,wprk->hwc", rows_back, pieces[chunk], preferred_element_type=jnp.float32
        )
    return total.astype(jnp.bfloat16)[None]


def solution(mesh):
    in_specs = (P("gop", "row", None, None), P(None, None, None, "row", None), P())
    out_specs = P("gop", "row", None, None)
    return jax.shard_map(
        on_device, mesh=mesh, in_specs=in_specs, out_specs=out_specs, check_vma=False
    )
```

```python
import math

import jax
import jax.numpy as jnp
from jax import lax
from jax.sharding import PartitionSpec as P


def row_table(length):
    across = jnp.arange(length, dtype=jnp.int32)
    phases = across[:, None] * across[None, :] % length
    angles = phases.astype(jnp.float32) * (2.0 * math.pi / length)
    factor = 1.0 / math.sqrt(length)
    return jnp.concatenate([jnp.cos(angles) * factor, -jnp.sin(angles) * factor], axis=1).astype(
        jnp.bfloat16
    )


def column_matrix(length, sign, row_of, col_of):
    rows = lax.broadcasted_iota(jnp.int32, (2 * length, 2 * length), 0)
    cols = lax.broadcasted_iota(jnp.int32, (2 * length, 2 * length), 1)
    k, p = row_of(rows)
    h, q = col_of(cols)
    phases = k * h % length
    angles = phases.astype(jnp.float32) * (2.0 * math.pi / length)
    factor = 1.0 / math.sqrt(length)
    cosine = jnp.cos(angles) * factor
    sine_part = sign * jnp.sin(angles) * factor
    value = jnp.where(p == q, cosine, jnp.where(p == 0, -sine_part, sine_part))
    return value.astype(jnp.bfloat16)


def interleaved(index):
    return index // 2, index % 2


def blocked(kb):
    def split(index):
        blk, rest = index // (2 * kb), index % (2 * kb)
        return blk * kb + rest % kb, rest // kb

    return split


CHUNKS = 3


def shifted(kb, frames, me, sign):
    def split(index):
        s, rest = index // (2 * kb), index % (2 * kb)
        return ((me + sign * s) % frames) * kb + rest % kb, rest // kb

    return split


def on_device(features, filters, anchors):
    frames = lax.psum(1, "gop")
    blocks = lax.psum(1, "row")
    _, hb, columns, chans = features.shape
    height = filters.shape[1]
    wb = columns // blocks
    kb = height // frames
    part = wb // CHUNKS
    lanes = part * chans
    me = lax.axis_index("gop")

    table = row_table(columns).reshape(columns, 2, blocks, wb)
    forward_cols = column_matrix(height, -1.0, shifted(kb, frames, me, 1), interleaved)
    inverse_cols = column_matrix(height, 1.0, interleaved, shifted(kb, frames, me, -1))
    shifts = [[(i, (i + s) % frames) for i in range(frames)] for s in range(frames)]

    x = features[0]
    gains = lax.dynamic_slice_in_dim(filters, me * kb, kb, axis=1)
    gains = gains.transpose(0, 2, 1, 3, 4)
    def mix(every, gain):
        outs = []
        for s in range(frames):
            frame = (me + s) % frames
            picks = (
                (me - frame) % frames,
                (me - anchors[frame, 0]) % frames,
                (me - anchors[frame, 1]) % frames,
            )
            sources = [lax.dynamic_index_in_dim(every, pick, 0, keepdims=False) for pick in picks]
            real_part = jnp.zeros((kb, lanes), jnp.float32)
            imag_part = jnp.zeros((kb, lanes), jnp.float32)
            for which_one in range(3):
                source_real = sources[which_one][0].astype(jnp.float32)
                source_imag = sources[which_one][1].astype(jnp.float32)
                gain_real = gain[which_one, 0]
                gain_imag = gain[which_one, 1]
                real_part = real_part + gain_real * source_real - gain_imag * source_imag
                imag_part = imag_part + gain_real * source_imag + gain_imag * source_real
            outs.append(jnp.stack([real_part, imag_part]).astype(jnp.bfloat16))
        return outs

    def exchange(pieces):
        return [pieces[0]] + [lax.ppermute(pieces[s], "gop", shifts[s]) for s in range(1, frames)]

    chunks = [slice(c * part, (c + 1) * part) for c in range(CHUNKS)]
    pieces = [table[:, :, :, cols] for cols in chunks]
    slabs = []
    for chunk in range(CHUNKS):
        rowwise = jnp.einsum(
            "hwc,wprk->rhpkc", x, pieces[chunk], preferred_element_type=jnp.float32
        ).astype(jnp.bfloat16)
        slabs.append(lax.all_to_all(rowwise, "row", 0, 0, tiled=True))
    everys = []
    for chunk in range(CHUNKS):
        spectra = jnp.dot(
            forward_cols, slabs[chunk].reshape(2 * height, lanes), preferred_element_type=jnp.float32
        ).astype(jnp.bfloat16)
        spectra = spectra.reshape(frames, 2, kb, lanes)
        if chunk:
            spectra, _ = lax.optimization_barrier((spectra, everys[-1]))
        everys.append(jnp.stack(exchange([spectra[s] for s in range(frames)])))
    mines = []
    for chunk in range(CHUNKS):
        gain = gains[:, :, :, chunks[chunk]].reshape(3, 2, kb, lanes).astype(jnp.float32)
        outs = mix(everys[chunk], gain)
        if chunk:
            outs, _ = lax.optimization_barrier((outs, mines[-1]))
        mines.append(jnp.stack(exchange(outs)))
    total = x.astype(jnp.float32)
    for chunk in range(CHUNKS):
        back = jnp.dot(
            inverse_cols, mines[chunk].reshape(2 * height, lanes), preferred_element_type=jnp.float32
        ).astype(jnp.bfloat16)
        back = back.reshape(blocks, 2 * hb, lanes)
        rows_back = lax.all_to_all(back, "row", 0, 0, tiled=True)
        rows_back = rows_back.reshape(blocks, hb, 2, part, chans)
        total = total + jnp.einsum(
            "rhpkc,wprk->hwc", rows_back, pieces[chunk], preferred_element_type=jnp.float32
        )
    return total.astype(jnp.bfloat16)[None]


def solution(mesh):
    in_specs = (P("gop", "row", None, None), P(None, None, None, "row", None), P())
    out_specs = P("gop", "row", None, None)
    return jax.shard_map(
        on_device, mesh=mesh, in_specs=in_specs, out_specs=out_specs, check_vma=False
    )
```

```python
import math

import jax
import jax.numpy as jnp
from jax import lax
from jax.sharding import PartitionSpec as P


def row_table(length):
    across = jnp.arange(length, dtype=jnp.int32)
    phases = across[:, None] * across[None, :] % length
    angles = phases.astype(jnp.float32) * (2.0 * math.pi / length)
    factor = 1.0 / math.sqrt(length)
    return jnp.concatenate([jnp.cos(angles) * factor, -jnp.sin(angles) * factor], axis=1).astype(
        jnp.bfloat16
    )


def column_matrix(length, sign, row_of, col_of, after):
    rows = lax.broadcasted_iota(jnp.int32, (2 * length, 2 * length), 0)
    cols = lax.broadcasted_iota(jnp.int32, (2 * length, 2 * length), 1)
    k, p = row_of(rows)
    h, q = col_of(cols)
    phases = k * h % length
    angles = phases.astype(jnp.float32) * (2.0 * math.pi / length) + 0.0 * after
    factor = 1.0 / math.sqrt(length)
    cosine = jnp.cos(angles) * factor
    sine_part = sign * jnp.sin(angles) * factor
    value = jnp.where(p == q, cosine, jnp.where(p == 0, -sine_part, sine_part))
    return value.astype(jnp.bfloat16)


def row_piece(length, blocks, start, width):
    w = lax.broadcasted_iota(jnp.int32, (length, blocks, width), 0)
    k = lax.broadcasted_iota(jnp.int32, (length, blocks, width), 1) * (length // blocks)
    k = k + start + lax.broadcasted_iota(jnp.int32, (length, blocks, width), 2)
    phases = w * k % length
    angles = phases.astype(jnp.float32) * (2.0 * math.pi / length)
    factor = 1.0 / math.sqrt(length)
    return jnp.stack([jnp.cos(angles) * factor, -jnp.sin(angles) * factor], axis=1).astype(jnp.bfloat16)


def interleaved(index):
    return index // 2, index % 2


def blocked(kb):
    def split(index):
        blk, rest = index // (2 * kb), index % (2 * kb)
        return blk * kb + rest % kb, rest // kb

    return split


CHUNKS = 2


def shifted(kb, frames, me, sign):
    def split(index):
        s, rest = index // (2 * kb), index % (2 * kb)
        return ((me + sign * s) % frames) * kb + rest % kb, rest // kb

    return split


def on_device(features, filters, anchors):
    frames = lax.psum(1, "gop")
    blocks = lax.psum(1, "row")
    _, hb, columns, chans = features.shape
    height = filters.shape[1]
    wb = columns // blocks
    kb = height // frames
    part = wb // CHUNKS
    lanes = part * chans
    me = lax.axis_index("gop")

    shifts = [[(i, (i + s) % frames) for i in range(frames)] for s in range(frames)]

    x = features[0]
    gains = lax.dynamic_slice_in_dim(filters, me * kb, kb, axis=1)
    gains = gains.transpose(0, 2, 1, 3, 4)
    def mix(every, gain):
        def one(s, done):
            frame = (me + s) % frames
            picks = (
                (me - frame) % frames,
                (me - anchors[frame, 0]) % frames,
                (me - anchors[frame, 1]) % frames,
            )
            sources = [lax.dynamic_index_in_dim(every, pick, 0, keepdims=False) for pick in picks]
            real_part = jnp.zeros((kb, lanes), jnp.float32)
            imag_part = jnp.zeros((kb, lanes), jnp.float32)
            for which_one in range(3):
                source_real = sources[which_one][0].astype(jnp.float32)
                source_imag = sources[which_one][1].astype(jnp.float32)
                gain_real = gain[which_one, 0]
                gain_imag = gain[which_one, 1]
                real_part = real_part + gain_real * source_real - gain_imag * source_imag
                imag_part = imag_part + gain_real * source_imag + gain_imag * source_real
            result = jnp.stack([real_part, imag_part]).astype(jnp.bfloat16)
            return lax.dynamic_update_index_in_dim(done, result, s, 0)

        done = lax.fori_loop(0, frames, one, jnp.zeros((frames, 2, kb, lanes), jnp.bfloat16))
        return [done[s] for s in range(frames)]

    def exchange(pieces):
        return [pieces[0]] + [lax.ppermute(pieces[s], "gop", shifts[s]) for s in range(1, frames)]

    chunks = [slice(c * part, (c + 1) * part) for c in range(CHUNKS)]
    pieces = [row_piece(columns, blocks, c * part, part) for c in range(CHUNKS)]
    slabs = []
    for chunk in range(CHUNKS):
        rowwise = jnp.einsum(
            "hwc,wprk->rhpkc", x, pieces[chunk], preferred_element_type=jnp.float32
        ).astype(jnp.bfloat16)
        if chunk == 0:
            after = rowwise[0, 0, 0, 0, 0].astype(jnp.float32)
        slabs.append(lax.all_to_all(rowwise, "row", 0, 0, tiled=True))
    forward_cols = column_matrix(height, -1.0, shifted(kb, frames, me, 1), interleaved, after)
    inverse_cols = column_matrix(height, 1.0, interleaved, shifted(kb, frames, me, -1), after)
    forward_cols, inverse_cols = lax.optimization_barrier((forward_cols, inverse_cols))
    everys = []
    for chunk in range(CHUNKS):
        spectra = jnp.dot(
            forward_cols, slabs[chunk].reshape(2 * height, lanes), preferred_element_type=jnp.float32
        ).astype(jnp.bfloat16)
        spectra = spectra.reshape(frames, 2, kb, lanes)
        if chunk:
            spectra, _ = lax.optimization_barrier((spectra, everys[-1]))
        everys.append(jnp.stack(exchange([spectra[s] for s in range(frames)])))
    mines = []
    for chunk in range(CHUNKS):
        gain = gains[:, :, :, chunks[chunk]].reshape(3, 2, kb, lanes).astype(jnp.float32)
        outs = mix(everys[chunk], gain)
        if chunk:
            outs, _ = lax.optimization_barrier((outs, mines[-1]))
        mines.append(jnp.stack(exchange(outs)))
    total = x.astype(jnp.float32)
    for chunk in range(CHUNKS):
        back = jnp.dot(
            inverse_cols, mines[chunk].reshape(2 * height, lanes), preferred_element_type=jnp.float32
        ).astype(jnp.bfloat16)
        back = back.reshape(blocks, 2 * hb, lanes)
        rows_back = lax.all_to_all(back, "row", 0, 0, tiled=True)
        rows_back = rows_back.reshape(blocks, hb, 2, part, chans)
        total = total + jnp.einsum(
            "rhpkc,wprk->hwc", rows_back, pieces[chunk], preferred_element_type=jnp.float32
        )
    return total.astype(jnp.bfloat16)[None]


def solution(mesh):
    in_specs = (P("gop", "row", None, None), P(None, None, None, "row", None), P())
    out_specs = P("gop", "row", None, None)
    return jax.shard_map(
        on_device, mesh=mesh, in_specs=in_specs, out_specs=out_specs, check_vma=False
    )
```

```python
import math

import jax
import jax.numpy as jnp
from jax import lax
from jax.sharding import PartitionSpec as P


def row_table(length):
    across = jnp.arange(length, dtype=jnp.int32)
    phases = across[:, None] * across[None, :] % length
    angles = phases.astype(jnp.float32) * (2.0 * math.pi / length)
    factor = 1.0 / math.sqrt(length)
    return jnp.concatenate([jnp.cos(angles) * factor, -jnp.sin(angles) * factor], axis=1).astype(
        jnp.bfloat16
    )


def column_matrix(length, sign, row_of, col_of, after):
    rows = lax.broadcasted_iota(jnp.int32, (2 * length, 2 * length), 0)
    cols = lax.broadcasted_iota(jnp.int32, (2 * length, 2 * length), 1)
    k, p = row_of(rows)
    h, q = col_of(cols)
    phases = k * h % length
    angles = phases.astype(jnp.float32) * (2.0 * math.pi / length) + 0.0 * after
    factor = 1.0 / math.sqrt(length)
    cosine = jnp.cos(angles) * factor
    sine_part = sign * jnp.sin(angles) * factor
    value = jnp.where(p == q, cosine, jnp.where(p == 0, -sine_part, sine_part))
    return value.astype(jnp.bfloat16)


def row_piece(length, blocks, start, width):
    w = lax.broadcasted_iota(jnp.int32, (length, blocks, width), 0)
    k = lax.broadcasted_iota(jnp.int32, (length, blocks, width), 1) * (length // blocks)
    k = k + start + lax.broadcasted_iota(jnp.int32, (length, blocks, width), 2)
    phases = w * k % length
    angles = phases.astype(jnp.float32) * (2.0 * math.pi / length)
    factor = 1.0 / math.sqrt(length)
    return jnp.stack([jnp.cos(angles) * factor, -jnp.sin(angles) * factor], axis=1).astype(jnp.bfloat16)


def interleaved(index):
    return index // 2, index % 2


def blocked(kb):
    def split(index):
        blk, rest = index // (2 * kb), index % (2 * kb)
        return blk * kb + rest % kb, rest // kb

    return split


CHUNKS = 2


def shifted(kb, frames, me, sign):
    def split(index):
        s, rest = index // (2 * kb), index % (2 * kb)
        return ((me + sign * s) % frames) * kb + rest % kb, rest // kb

    return split


def on_device(features, filters, anchors):
    frames = lax.psum(1, "gop")
    blocks = lax.psum(1, "row")
    _, hb, columns, chans = features.shape
    height = filters.shape[1]
    wb = columns // blocks
    kb = height // frames
    part = wb // CHUNKS
    lanes = part * chans
    me = lax.axis_index("gop")

    shifts = [[(i, (i + s) % frames) for i in range(frames)] for s in range(frames)]

    x = features[0]
    gains = lax.dynamic_slice_in_dim(filters, me * kb, kb, axis=1)
    gains = gains.transpose(0, 2, 1, 3, 4)
    def mix(every, gain):
        outs = []
        for s in range(frames):
            frame = (me + s) % frames
            picks = (
                (me - frame) % frames,
                (me - anchors[frame, 0]) % frames,
                (me - anchors[frame, 1]) % frames,
            )
            sources = [lax.dynamic_index_in_dim(every, pick, 0, keepdims=False) for pick in picks]
            real_part = jnp.zeros((kb, lanes), jnp.float32)
            imag_part = jnp.zeros((kb, lanes), jnp.float32)
            for which_one in range(3):
                source_real = sources[which_one][0].astype(jnp.float32)
                source_imag = sources[which_one][1].astype(jnp.float32)
                gain_real = gain[which_one, 0]
                gain_imag = gain[which_one, 1]
                real_part = real_part + gain_real * source_real - gain_imag * source_imag
                imag_part = imag_part + gain_real * source_imag + gain_imag * source_real
            outs.append(jnp.stack([real_part, imag_part]).astype(jnp.bfloat16))
        return outs

    def exchange(pieces):
        return [pieces[0]] + [lax.ppermute(pieces[s], "gop", shifts[s]) for s in range(1, frames)]

    chunks = [slice(c * part, (c + 1) * part) for c in range(CHUNKS)]
    pieces = [row_piece(columns, blocks, c * part, part) for c in range(CHUNKS)]
    slabs = []
    for chunk in range(CHUNKS):
        rowwise = jnp.einsum(
            "hwc,wprk->rhpkc", x, pieces[chunk], preferred_element_type=jnp.float32
        ).astype(jnp.bfloat16)
        if chunk == 0:
            after = rowwise[0, 0, 0, 0, 0].astype(jnp.float32)
        slabs.append(lax.all_to_all(rowwise, "row", 0, 0, tiled=True))
    natural = column_matrix(height, -1.0, blocked(kb), interleaved, after).reshape(frames, 2 * kb, 2 * height)
    order = lax.broadcasted_iota(jnp.int32, (frames,), 0)
    forward_cols = jnp.take(natural, (me + order) % frames, axis=0).reshape(2 * height, 2 * height)
    inverse_cols = jnp.take(natural, (me - order) % frames, axis=0).reshape(2 * height, 2 * height).T
    forward_cols, inverse_cols = lax.optimization_barrier((forward_cols, inverse_cols))
    everys = []
    for chunk in range(CHUNKS):
        spectra = jnp.dot(
            forward_cols, slabs[chunk].reshape(2 * height, lanes), preferred_element_type=jnp.float32
        ).astype(jnp.bfloat16)
        spectra = spectra.reshape(frames, 2, kb, lanes)
        if chunk:
            spectra, _ = lax.optimization_barrier((spectra, everys[-1]))
        everys.append(jnp.stack(exchange([spectra[s] for s in range(frames)])))
    mines = []
    for chunk in range(CHUNKS):
        gain = gains[:, :, :, chunks[chunk]].reshape(3, 2, kb, lanes).astype(jnp.float32)
        outs = mix(everys[chunk], gain)
        if chunk:
            outs, _ = lax.optimization_barrier((outs, mines[-1]))
        mines.append(jnp.stack(exchange(outs)))
    total = x.astype(jnp.float32)
    for chunk in range(CHUNKS):
        back = jnp.dot(
            inverse_cols, mines[chunk].reshape(2 * height, lanes), preferred_element_type=jnp.float32
        ).astype(jnp.bfloat16)
        back = back.reshape(blocks, 2 * hb, lanes)
        rows_back = lax.all_to_all(back, "row", 0, 0, tiled=True)
        rows_back = rows_back.reshape(blocks, hb, 2, part, chans)
        total = total + jnp.einsum(
            "rhpkc,wprk->hwc", rows_back, pieces[chunk], preferred_element_type=jnp.float32
        )
    return total.astype(jnp.bfloat16)[None]


def solution(mesh):
    in_specs = (P("gop", "row", None, None), P(None, None, None, "row", None), P())
    out_specs = P("gop", "row", None, None)
    return jax.shard_map(
        on_device, mesh=mesh, in_specs=in_specs, out_specs=out_specs, check_vma=False
    )
```

```python
import math

import jax
import jax.numpy as jnp
from jax import lax
from jax.sharding import PartitionSpec as P


def row_table(length):
    across = jnp.arange(length, dtype=jnp.int32)
    phases = across[:, None] * across[None, :] % length
    angles = phases.astype(jnp.float32) * (2.0 * math.pi / length)
    factor = 1.0 / math.sqrt(length)
    return jnp.concatenate([jnp.cos(angles) * factor, -jnp.sin(angles) * factor], axis=1).astype(
        jnp.bfloat16
    )


def column_matrix(length, sign, row_of, col_of, after):
    rows = lax.broadcasted_iota(jnp.int32, (2 * length, 2 * length), 0)
    cols = lax.broadcasted_iota(jnp.int32, (2 * length, 2 * length), 1)
    k, p = row_of(rows)
    h, q = col_of(cols)
    phases = k * h % length
    angles = phases.astype(jnp.float32) * (2.0 * math.pi / length) + 0.0 * after
    factor = 1.0 / math.sqrt(length)
    cosine = jnp.cos(angles) * factor
    sine_part = sign * jnp.sin(angles) * factor
    value = jnp.where(p == q, cosine, jnp.where(p == 0, -sine_part, sine_part))
    return value.astype(jnp.bfloat16)


def row_piece(length, blocks, start, width):
    w = lax.broadcasted_iota(jnp.int32, (length, blocks, width), 0)
    k = lax.broadcasted_iota(jnp.int32, (length, blocks, width), 1) * (length // blocks)
    k = k + start + lax.broadcasted_iota(jnp.int32, (length, blocks, width), 2)
    phases = w * k % length
    angles = phases.astype(jnp.float32) * (2.0 * math.pi / length)
    factor = 1.0 / math.sqrt(length)
    return jnp.stack([jnp.cos(angles) * factor, -jnp.sin(angles) * factor], axis=1).astype(jnp.bfloat16)


def interleaved(index):
    return index // 2, index % 2


def blocked(kb):
    def split(index):
        blk, rest = index // (2 * kb), index % (2 * kb)
        return blk * kb + rest % kb, rest // kb

    return split


CHUNKS = 2


def shifted(kb, frames, me, sign):
    def split(index):
        s, rest = index // (2 * kb), index % (2 * kb)
        return ((me + sign * s) % frames) * kb + rest % kb, rest // kb

    return split


def on_device(features, filters, anchors):
    frames = lax.psum(1, "gop")
    blocks = lax.psum(1, "row")
    _, hb, columns, chans = features.shape
    height = filters.shape[1]
    wb = columns // blocks
    kb = height // frames
    part = wb // CHUNKS
    lanes = part * chans
    me = lax.axis_index("gop")

    shifts = [[(i, (i + s) % frames) for i in range(frames)] for s in range(frames)]

    x = features[0]
    gains = lax.dynamic_slice_in_dim(filters, me * kb, kb, axis=1)
    gains = gains.transpose(0, 2, 1, 3, 4)
    def mix(every, gain):
        outs = []
        for s in range(frames):
            frame = (me + s) % frames
            picks = (
                (me - frame) % frames,
                (me - anchors[frame, 0]) % frames,
                (me - anchors[frame, 1]) % frames,
            )
            sources = [lax.dynamic_index_in_dim(every, pick, 0, keepdims=False) for pick in picks]
            real_part = jnp.zeros((kb, lanes), jnp.float32)
            imag_part = jnp.zeros((kb, lanes), jnp.float32)
            for which_one in range(3):
                source_real = sources[which_one][0].astype(jnp.float32)
                source_imag = sources[which_one][1].astype(jnp.float32)
                gain_real = gain[which_one, 0]
                gain_imag = gain[which_one, 1]
                real_part = real_part + gain_real * source_real - gain_imag * source_imag
                imag_part = imag_part + gain_real * source_imag + gain_imag * source_real
            outs.append(jnp.stack([real_part, imag_part]).astype(jnp.bfloat16))
        return outs

    def exchange(pieces):
        return [pieces[0]] + [lax.ppermute(pieces[s], "gop", shifts[s]) for s in range(1, frames)]

    chunks = [slice(c * part, (c + 1) * part) for c in range(CHUNKS)]
    pieces = [row_piece(columns, blocks, c * part, part) for c in range(CHUNKS)]
    def row_transform(chunk):
        return jnp.einsum(
            "hwc,wprk->rhpkc", x, pieces[chunk], preferred_element_type=jnp.float32
        ).astype(jnp.bfloat16)

    def column_transform(slab):
        spectra = jnp.dot(
            forward_cols, slab.reshape(2 * height, lanes), preferred_element_type=jnp.float32
        ).astype(jnp.bfloat16)
        return spectra.reshape(frames, 2, kb, lanes)

    rowwise = row_transform(0)
    after = rowwise[0, 0, 0, 0, 0].astype(jnp.float32)
    slabs = [lax.all_to_all(rowwise, "row", 0, 0, tiled=True)]
    natural = column_matrix(height, -1.0, blocked(kb), interleaved, after).reshape(frames, 2 * kb, 2 * height)
    order = lax.broadcasted_iota(jnp.int32, (frames,), 0)
    forward_cols = jnp.take(natural, (me + order) % frames, axis=0).reshape(2 * height, 2 * height)
    inverse_cols = jnp.take(natural, (me - order) % frames, axis=0).reshape(2 * height, 2 * height).T
    forward_cols, inverse_cols = lax.optimization_barrier((forward_cols, inverse_cols))
    everys = []
    for chunk in range(CHUNKS):
        spectra = column_transform(slabs[chunk])
        if chunk + 1 < CHUNKS:
            rowwise, spectra = lax.optimization_barrier((row_transform(chunk + 1), spectra))
            slabs.append(lax.all_to_all(rowwise, "row", 0, 0, tiled=True))
        if chunk:
            spectra, _ = lax.optimization_barrier((spectra, everys[-1]))
        everys.append(jnp.stack(exchange([spectra[s] for s in range(frames)])))
    mines = []
    for chunk in range(CHUNKS):
        gain = gains[:, :, :, chunks[chunk]].reshape(3, 2, kb, lanes).astype(jnp.float32)
        outs = mix(everys[chunk], gain)
        if chunk:
            outs, _ = lax.optimization_barrier((outs, mines[-1]))
        mines.append(jnp.stack(exchange(outs)))
    total = x.astype(jnp.float32)
    for chunk in range(CHUNKS):
        back = jnp.dot(
            inverse_cols, mines[chunk].reshape(2 * height, lanes), preferred_element_type=jnp.float32
        ).astype(jnp.bfloat16)
        back = back.reshape(blocks, 2 * hb, lanes)
        rows_back = lax.all_to_all(back, "row", 0, 0, tiled=True)
        rows_back = rows_back.reshape(blocks, hb, 2, part, chans)
        total = total + jnp.einsum(
            "rhpkc,wprk->hwc", rows_back, pieces[chunk], preferred_element_type=jnp.float32
        )
    return total.astype(jnp.bfloat16)[None]


def solution(mesh):
    in_specs = (P("gop", "row", None, None), P(None, None, None, "row", None), P())
    out_specs = P("gop", "row", None, None)
    return jax.shard_map(
        on_device, mesh=mesh, in_specs=in_specs, out_specs=out_specs, check_vma=False
    )
```

```python
import math

import jax
import jax.numpy as jnp
from jax import lax
from jax.sharding import PartitionSpec as P


def row_table(length):
    across = jnp.arange(length, dtype=jnp.int32)
    phases = across[:, None] * across[None, :] % length
    angles = phases.astype(jnp.float32) * (2.0 * math.pi / length)
    factor = 1.0 / math.sqrt(length)
    return jnp.concatenate([jnp.cos(angles) * factor, -jnp.sin(angles) * factor], axis=1).astype(
        jnp.bfloat16
    )


def column_matrix(length, sign, row_of, col_of, after):
    rows = lax.broadcasted_iota(jnp.int32, (2 * length, 2 * length), 0)
    cols = lax.broadcasted_iota(jnp.int32, (2 * length, 2 * length), 1)
    k, p = row_of(rows)
    h, q = col_of(cols)
    phases = k * h % length
    angles = phases.astype(jnp.float32) * (2.0 * math.pi / length) + 0.0 * after
    factor = 1.0 / math.sqrt(length)
    cosine = jnp.cos(angles) * factor
    sine_part = sign * jnp.sin(angles) * factor
    value = jnp.where(p == q, cosine, jnp.where(p == 0, -sine_part, sine_part))
    return value.astype(jnp.bfloat16)


def row_piece(length, blocks, start, width):
    w = lax.broadcasted_iota(jnp.int32, (length, blocks, width), 0)
    k = lax.broadcasted_iota(jnp.int32, (length, blocks, width), 1) * (length // blocks)
    k = k + start + lax.broadcasted_iota(jnp.int32, (length, blocks, width), 2)
    phases = w * k % length
    angles = phases.astype(jnp.float32) * (2.0 * math.pi / length)
    factor = 1.0 / math.sqrt(length)
    return jnp.stack([jnp.cos(angles) * factor, -jnp.sin(angles) * factor], axis=1).astype(jnp.bfloat16)


def interleaved(index):
    return index // 2, index % 2


def blocked(kb):
    def split(index):
        blk, rest = index // (2 * kb), index % (2 * kb)
        return blk * kb + rest % kb, rest // kb

    return split


CHUNKS = 2


def shifted(kb, frames, me, sign):
    def split(index):
        s, rest = index // (2 * kb), index % (2 * kb)
        return ((me + sign * s) % frames) * kb + rest % kb, rest // kb

    return split


def on_device(features, filters, anchors):
    frames = lax.psum(1, "gop")
    blocks = lax.psum(1, "row")
    _, hb, columns, chans = features.shape
    height = filters.shape[1]
    wb = columns // blocks
    kb = height // frames
    part = wb // CHUNKS
    lanes = part * chans
    me = lax.axis_index("gop")

    chips = frames // 2
    z, core = me // 2, me % 2

    def at(zz, cc):
        return 2 * (zz % chips) + cc

    target = [me, at(z, 1 - core), at(z + 1, core), at(z + 1, 1 - core), at(z - 1, core),
              at(z - 1, 1 - core), at(z + 2, core), at(z + 2, 1 - core)]
    source = [me, at(z, 1 - core), at(z - 1, core), at(z - 1, 1 - core), at(z + 1, core),
              at(z + 1, 1 - core), at(z + 2, core), at(z + 2, 1 - core)]
    target = jnp.stack([jnp.asarray(t, jnp.int32) for t in target])
    source = jnp.stack([jnp.asarray(t, jnp.int32) for t in source])
    slot_of = sum(t * (lax.broadcasted_iota(jnp.int32, (frames,), 0) == source[t]) for t in range(frames))

    def moves(step_z, flip):
        return [(at(zz, cc), at(zz + step_z, (cc + flip) % 2)) for zz in range(chips) for cc in range(2)]

    swap, up, up_x, down, down_x = moves(0, 1), moves(1, 0), moves(1, 1), moves(-1, 0), moves(-1, 1)

    x = features[0]
    gains = lax.dynamic_slice_in_dim(filters, me * kb, kb, axis=1)
    gains = gains.transpose(0, 2, 1, 3, 4)
    def mix(every, gain):
        outs = []
        for t in range(frames):
            frame = target[t]
            picks = (slot_of[frame], slot_of[anchors[frame, 0]], slot_of[anchors[frame, 1]])
            sources = [lax.dynamic_index_in_dim(every, pick, 0, keepdims=False) for pick in picks]
            real_part = jnp.zeros((kb, lanes), jnp.float32)
            imag_part = jnp.zeros((kb, lanes), jnp.float32)
            for which_one in range(3):
                source_real = sources[which_one][0].astype(jnp.float32)
                source_imag = sources[which_one][1].astype(jnp.float32)
                gain_real = gain[which_one, 0]
                gain_imag = gain[which_one, 1]
                real_part = real_part + gain_real * source_real - gain_imag * source_imag
                imag_part = imag_part + gain_real * source_imag + gain_imag * source_real
            outs.append(jnp.stack([real_part, imag_part]).astype(jnp.bfloat16))
        return outs

    def exchange(pieces):
        send = lambda value, plan: lax.ppermute(value, "gop", plan)
        return [
            pieces[0],
            send(pieces[1], swap),
            send(pieces[2], up),
            send(pieces[3], up_x),
            send(pieces[4], down),
            send(pieces[5], down_x),
            send(send(pieces[6], up), up),
            send(send(pieces[7], down), down_x),
        ]

    chunks = [slice(c * part, (c + 1) * part) for c in range(CHUNKS)]
    pieces = [row_piece(columns, blocks, c * part, part) for c in range(CHUNKS)]
    def row_transform(chunk):
        return jnp.einsum(
            "hwc,wprk->rhpkc", x, pieces[chunk], preferred_element_type=jnp.float32
        ).astype(jnp.bfloat16)

    def column_transform(slab):
        spectra = jnp.dot(
            forward_cols, slab.reshape(2 * height, lanes), preferred_element_type=jnp.float32
        ).astype(jnp.bfloat16)
        return spectra.reshape(frames, 2, kb, lanes)

    rowwise = row_transform(0)
    after = rowwise[0, 0, 0, 0, 0].astype(jnp.float32)
    slabs = [lax.all_to_all(rowwise, "row", 0, 0, tiled=True)]
    natural = column_matrix(height, -1.0, blocked(kb), interleaved, after).reshape(frames, 2 * kb, 2 * height)
    forward_cols = jnp.take(natural, target, axis=0).reshape(2 * height, 2 * height)
    inverse_cols = jnp.take(natural, source, axis=0).reshape(2 * height, 2 * height).T
    forward_cols, inverse_cols = lax.optimization_barrier((forward_cols, inverse_cols))
    everys = []
    for chunk in range(CHUNKS):
        spectra = column_transform(slabs[chunk])
        if chunk + 1 < CHUNKS:
            rowwise, spectra = lax.optimization_barrier((row_transform(chunk + 1), spectra))
            slabs.append(lax.all_to_all(rowwise, "row", 0, 0, tiled=True))
        if chunk:
            spectra, _ = lax.optimization_barrier((spectra, everys[-1]))
        everys.append(jnp.stack(exchange([spectra[s] for s in range(frames)])))
    mines = []
    for chunk in range(CHUNKS):
        gain = gains[:, :, :, chunks[chunk]].reshape(3, 2, kb, lanes).astype(jnp.float32)
        outs = mix(everys[chunk], gain)
        if chunk:
            outs, _ = lax.optimization_barrier((outs, mines[-1]))
        mines.append(jnp.stack(exchange(outs)))
    total = x.astype(jnp.float32)
    for chunk in range(CHUNKS):
        back = jnp.dot(
            inverse_cols, mines[chunk].reshape(2 * height, lanes), preferred_element_type=jnp.float32
        ).astype(jnp.bfloat16)
        back = back.reshape(blocks, 2 * hb, lanes)
        rows_back = lax.all_to_all(back, "row", 0, 0, tiled=True)
        rows_back = rows_back.reshape(blocks, hb, 2, part, chans)
        total = total + jnp.einsum(
            "rhpkc,wprk->hwc", rows_back, pieces[chunk], preferred_element_type=jnp.float32
        )
    return total.astype(jnp.bfloat16)[None]


def solution(mesh):
    in_specs = (P("gop", "row", None, None), P(None, None, None, "row", None), P())
    out_specs = P("gop", "row", None, None)
    return jax.shard_map(
        on_device, mesh=mesh, in_specs=in_specs, out_specs=out_specs, check_vma=False
    )
```

```python
import math

import jax
import jax.numpy as jnp
from jax import lax
from jax.sharding import PartitionSpec as P


def row_table(length):
    across = jnp.arange(length, dtype=jnp.int32)
    phases = across[:, None] * across[None, :] % length
    angles = phases.astype(jnp.float32) * (2.0 * math.pi / length)
    factor = 1.0 / math.sqrt(length)
    return jnp.concatenate([jnp.cos(angles) * factor, -jnp.sin(angles) * factor], axis=1).astype(
        jnp.bfloat16
    )


def column_matrix(length, sign, row_of, col_of, after):
    rows = lax.broadcasted_iota(jnp.int32, (2 * length, 2 * length), 0)
    cols = lax.broadcasted_iota(jnp.int32, (2 * length, 2 * length), 1)
    k, p = row_of(rows)
    h, q = col_of(cols)
    phases = k * h % length
    angles = phases.astype(jnp.float32) * (2.0 * math.pi / length) + 0.0 * after
    factor = 1.0 / math.sqrt(length)
    cosine = jnp.cos(angles) * factor
    sine_part = sign * jnp.sin(angles) * factor
    value = jnp.where(p == q, cosine, jnp.where(p == 0, -sine_part, sine_part))
    return value.astype(jnp.bfloat16)


def row_piece(length, blocks, start, width):
    w = lax.broadcasted_iota(jnp.int32, (length, blocks, width), 0)
    k = lax.broadcasted_iota(jnp.int32, (length, blocks, width), 1) * (length // blocks)
    k = k + start + lax.broadcasted_iota(jnp.int32, (length, blocks, width), 2)
    phases = w * k % length
    angles = phases.astype(jnp.float32) * (2.0 * math.pi / length)
    factor = 1.0 / math.sqrt(length)
    return jnp.stack([jnp.cos(angles) * factor, -jnp.sin(angles) * factor], axis=1).astype(jnp.bfloat16)


def interleaved(index):
    return index // 2, index % 2


def blocked(kb):
    def split(index):
        blk, rest = index // (2 * kb), index % (2 * kb)
        return blk * kb + rest % kb, rest // kb

    return split


CHUNKS = 2


def shifted(kb, frames, me, sign):
    def split(index):
        s, rest = index // (2 * kb), index % (2 * kb)
        return ((me + sign * s) % frames) * kb + rest % kb, rest // kb

    return split


def on_device(features, filters, anchors):
    frames = lax.psum(1, "gop")
    blocks = lax.psum(1, "row")
    _, hb, columns, chans = features.shape
    height = filters.shape[1]
    wb = columns // blocks
    kb = height // frames
    part = wb // CHUNKS
    lanes = part * chans
    me = lax.axis_index("gop")

    shifts = [[(i, (i + s) % frames) for i in range(frames)] for s in range(frames)]

    x = features[0]
    gains = lax.dynamic_slice_in_dim(filters, me * kb, kb, axis=1)
    gains = gains.transpose(0, 2, 1, 3, 4)
    def mix(every, gain):
        outs = []
        for s in range(frames):
            frame = (me + s) % frames
            picks = (
                (me - frame) % frames,
                (me - anchors[frame, 0]) % frames,
                (me - anchors[frame, 1]) % frames,
            )
            sources = [lax.dynamic_index_in_dim(every, pick, 0, keepdims=False) for pick in picks]
            real_part = jnp.zeros((kb, lanes), jnp.float32)
            imag_part = jnp.zeros((kb, lanes), jnp.float32)
            for which_one in range(3):
                source_real = sources[which_one][0].astype(jnp.float32)
                source_imag = sources[which_one][1].astype(jnp.float32)
                gain_real = gain[which_one, 0]
                gain_imag = gain[which_one, 1]
                real_part = real_part + gain_real * source_real - gain_imag * source_imag
                imag_part = imag_part + gain_real * source_imag + gain_imag * source_real
            outs.append(jnp.stack([real_part, imag_part]).astype(jnp.bfloat16))
        return outs

    def exchange(pieces):
        out = [pieces[0]]
        for s in range(1, frames):
            if 2 * s == frames:
                half = kb // 2
                ahead = pieces[s][:, :half]
                behind = pieces[s][:, half:]
                for step in (s // 2, frames - s // 2):
                    if step == s // 2:
                        ahead = lax.ppermute(lax.ppermute(ahead, "gop", shifts[step]), "gop", shifts[step])
                    else:
                        behind = lax.ppermute(lax.ppermute(behind, "gop", shifts[step]), "gop", shifts[step])
                out.append(jnp.concatenate([ahead, behind], axis=1))
            else:
                out.append(lax.ppermute(pieces[s], "gop", shifts[s]))
        return out

    chunks = [slice(c * part, (c + 1) * part) for c in range(CHUNKS)]
    pieces = [row_piece(columns, blocks, c * part, part) for c in range(CHUNKS)]
    def row_transform(chunk):
        return jnp.einsum(
            "hwc,wprk->rhpkc", x, pieces[chunk], preferred_element_type=jnp.float32
        ).astype(jnp.bfloat16)

    def column_transform(slab):
        spectra = jnp.dot(
            forward_cols, slab.reshape(2 * height, lanes), preferred_element_type=jnp.float32
        ).astype(jnp.bfloat16)
        return spectra.reshape(frames, 2, kb, lanes)

    rowwise = row_transform(0)
    after = rowwise[0, 0, 0, 0, 0].astype(jnp.float32)
    slabs = [lax.all_to_all(rowwise, "row", 0, 0, tiled=True)]
    natural = column_matrix(height, -1.0, blocked(kb), interleaved, after).reshape(frames, 2 * kb, 2 * height)
    order = lax.broadcasted_iota(jnp.int32, (frames,), 0)
    forward_cols = jnp.take(natural, (me + order) % frames, axis=0).reshape(2 * height, 2 * height)
    inverse_cols = jnp.take(natural, (me - order) % frames, axis=0).reshape(2 * height, 2 * height).T
    forward_cols, inverse_cols = lax.optimization_barrier((forward_cols, inverse_cols))
    everys = []
    for chunk in range(CHUNKS):
        spectra = column_transform(slabs[chunk])
        if chunk + 1 < CHUNKS:
            rowwise, spectra = lax.optimization_barrier((row_transform(chunk + 1), spectra))
            slabs.append(lax.all_to_all(rowwise, "row", 0, 0, tiled=True))
        if chunk:
            spectra, _ = lax.optimization_barrier((spectra, everys[-1]))
        everys.append(jnp.stack(exchange([spectra[s] for s in range(frames)])))
    mines = []
    for chunk in range(CHUNKS):
        gain = gains[:, :, :, chunks[chunk]].reshape(3, 2, kb, lanes).astype(jnp.float32)
        outs = mix(everys[chunk], gain)
        if chunk:
            outs, _ = lax.optimization_barrier((outs, mines[-1]))
        mines.append(jnp.stack(exchange(outs)))
    total = x.astype(jnp.float32)
    for chunk in range(CHUNKS):
        back = jnp.dot(
            inverse_cols, mines[chunk].reshape(2 * height, lanes), preferred_element_type=jnp.float32
        ).astype(jnp.bfloat16)
        back = back.reshape(blocks, 2 * hb, lanes)
        rows_back = lax.all_to_all(back, "row", 0, 0, tiled=True)
        rows_back = rows_back.reshape(blocks, hb, 2, part, chans)
        total = total + jnp.einsum(
            "rhpkc,wprk->hwc", rows_back, pieces[chunk], preferred_element_type=jnp.float32
        )
    return total.astype(jnp.bfloat16)[None]


def solution(mesh):
    in_specs = (P("gop", "row", None, None), P(None, None, None, "row", None), P())
    out_specs = P("gop", "row", None, None)
    return jax.shard_map(
        on_device, mesh=mesh, in_specs=in_specs, out_specs=out_specs, check_vma=False
    )
```

```python
import math

import jax
import jax.numpy as jnp
from jax import lax
from jax.sharding import PartitionSpec as P


def row_table(length):
    across = jnp.arange(length, dtype=jnp.int32)
    phases = across[:, None] * across[None, :] % length
    angles = phases.astype(jnp.float32) * (2.0 * math.pi / length)
    factor = 1.0 / math.sqrt(length)
    return jnp.concatenate([jnp.cos(angles) * factor, -jnp.sin(angles) * factor], axis=1).astype(
        jnp.bfloat16
    )


def column_matrix(length, sign, row_of, col_of, after):
    rows = lax.broadcasted_iota(jnp.int32, (2 * length, 2 * length), 0)
    cols = lax.broadcasted_iota(jnp.int32, (2 * length, 2 * length), 1)
    k, p = row_of(rows)
    h, q = col_of(cols)
    phases = k * h % length
    angles = phases.astype(jnp.float32) * (2.0 * math.pi / length) + 0.0 * after
    factor = 1.0 / math.sqrt(length)
    cosine = jnp.cos(angles) * factor
    sine_part = sign * jnp.sin(angles) * factor
    value = jnp.where(p == q, cosine, jnp.where(p == 0, -sine_part, sine_part))
    return value.astype(jnp.bfloat16)


def row_piece(length, blocks, start, width):
    w = lax.broadcasted_iota(jnp.int32, (length, blocks, width), 0)
    k = lax.broadcasted_iota(jnp.int32, (length, blocks, width), 1) * (length // blocks)
    k = k + start + lax.broadcasted_iota(jnp.int32, (length, blocks, width), 2)
    phases = w * k % length
    angles = phases.astype(jnp.float32) * (2.0 * math.pi / length)
    factor = 1.0 / math.sqrt(length)
    return jnp.stack([jnp.cos(angles) * factor, -jnp.sin(angles) * factor], axis=1).astype(jnp.bfloat16)


def interleaved(index):
    return index // 2, index % 2


def blocked(kb):
    def split(index):
        blk, rest = index // (2 * kb), index % (2 * kb)
        return blk * kb + rest % kb, rest // kb

    return split


CHUNKS = 3


def shifted(kb, frames, me, sign):
    def split(index):
        s, rest = index // (2 * kb), index % (2 * kb)
        return ((me + sign * s) % frames) * kb + rest % kb, rest // kb

    return split


def on_device(features, filters, anchors):
    frames = lax.psum(1, "gop")
    blocks = lax.psum(1, "row")
    _, hb, columns, chans = features.shape
    height = filters.shape[1]
    wb = columns // blocks
    kb = height // frames
    part = wb // CHUNKS
    lanes = part * chans
    me = lax.axis_index("gop")

    shifts = [[(i, (i + s) % frames) for i in range(frames)] for s in range(frames)]

    x = features[0]
    gains = lax.dynamic_slice_in_dim(filters, me * kb, kb, axis=1)
    gains = gains.transpose(0, 2, 1, 3, 4)
    def mix(every, gain):
        outs = []
        for s in range(frames):
            frame = (me + s) % frames
            picks = (
                (me - frame) % frames,
                (me - anchors[frame, 0]) % frames,
                (me - anchors[frame, 1]) % frames,
            )
            sources = [lax.dynamic_index_in_dim(every, pick, 0, keepdims=False) for pick in picks]
            real_part = jnp.zeros((kb, lanes), jnp.float32)
            imag_part = jnp.zeros((kb, lanes), jnp.float32)
            for which_one in range(3):
                source_real = sources[which_one][0].astype(jnp.float32)
                source_imag = sources[which_one][1].astype(jnp.float32)
                gain_real = gain[which_one, 0]
                gain_imag = gain[which_one, 1]
                real_part = real_part + gain_real * source_real - gain_imag * source_imag
                imag_part = imag_part + gain_real * source_imag + gain_imag * source_real
            outs.append(jnp.stack([real_part, imag_part]).astype(jnp.bfloat16))
        return outs

    def exchange(pieces):
        return [pieces[0]] + [lax.ppermute(pieces[s], "gop", shifts[s]) for s in range(1, frames)]

    chunks = [slice(c * part, (c + 1) * part) for c in range(CHUNKS)]
    pieces = [row_piece(columns, blocks, c * part, part) for c in range(CHUNKS)]
    def row_transform(chunk):
        return jnp.einsum(
            "hwc,wprk->rhpkc", x, pieces[chunk], preferred_element_type=jnp.float32
        ).astype(jnp.bfloat16)

    def column_transform(slab):
        spectra = jnp.dot(
            forward_cols, slab.reshape(2 * height, lanes), preferred_element_type=jnp.float32
        ).astype(jnp.bfloat16)
        return spectra.reshape(frames, 2, kb, lanes)

    rowwise = row_transform(0)
    after = rowwise[0, 0, 0, 0, 0].astype(jnp.float32)
    slabs = [lax.all_to_all(rowwise, "row", 0, 0, tiled=True)]
    natural = column_matrix(height, -1.0, blocked(kb), interleaved, after).reshape(frames, 2 * kb, 2 * height)
    order = lax.broadcasted_iota(jnp.int32, (frames,), 0)
    forward_cols = jnp.take(natural, (me + order) % frames, axis=0).reshape(2 * height, 2 * height)
    inverse_cols = jnp.take(natural, (me - order) % frames, axis=0).reshape(2 * height, 2 * height).T
    forward_cols, inverse_cols = lax.optimization_barrier((forward_cols, inverse_cols))
    everys = []
    for chunk in range(CHUNKS):
        spectra = column_transform(slabs[chunk])
        if chunk + 1 < CHUNKS:
            rowwise, spectra = lax.optimization_barrier((row_transform(chunk + 1), spectra))
            slabs.append(lax.all_to_all(rowwise, "row", 0, 0, tiled=True))
        if chunk:
            spectra, _ = lax.optimization_barrier((spectra, everys[-1]))
        everys.append(jnp.stack(exchange([spectra[s] for s in range(frames)])))
    mines = []
    for chunk in range(CHUNKS):
        gain = gains[:, :, :, chunks[chunk]].reshape(3, 2, kb, lanes).astype(jnp.float32)
        outs = mix(everys[chunk], gain)
        if chunk:
            outs, _ = lax.optimization_barrier((outs, mines[-1]))
        mines.append(jnp.stack(exchange(outs)))
    total = x.astype(jnp.float32)
    for chunk in range(CHUNKS):
        back = jnp.dot(
            inverse_cols, mines[chunk].reshape(2 * height, lanes), preferred_element_type=jnp.float32
        ).astype(jnp.bfloat16)
        back = back.reshape(blocks, 2 * hb, lanes)
        rows_back = lax.all_to_all(back, "row", 0, 0, tiled=True)
        rows_back = rows_back.reshape(blocks, hb, 2, part, chans)
        total = total + jnp.einsum(
            "rhpkc,wprk->hwc", rows_back, pieces[chunk], preferred_element_type=jnp.float32
        )
    return total.astype(jnp.bfloat16)[None]


def solution(mesh):
    in_specs = (P("gop", "row", None, None), P(None, None, None, "row", None), P())
    out_specs = P("gop", "row", None, None)
    return jax.shard_map(
        on_device, mesh=mesh, in_specs=in_specs, out_specs=out_specs, check_vma=False
    )
```

```python
import math

import jax
import jax.numpy as jnp
from jax import lax
from jax.sharding import PartitionSpec as P


def column_matrix(length, sign, row_of, col_of, after):
    rows = lax.broadcasted_iota(jnp.int32, (2 * length, 2 * length), 0)
    cols = lax.broadcasted_iota(jnp.int32, (2 * length, 2 * length), 1)
    k, p = row_of(rows)
    h, q = col_of(cols)
    phases = k * h % length
    angles = phases.astype(jnp.float32) * (2.0 * math.pi / length) + 0.0 * after
    factor = 1.0 / math.sqrt(length)
    cosine = jnp.cos(angles) * factor
    sine_part = sign * jnp.sin(angles) * factor
    value = jnp.where(p == q, cosine, jnp.where(p == 0, -sine_part, sine_part))
    return value.astype(jnp.bfloat16)


def row_piece(length, blocks, start, width):
    w = lax.broadcasted_iota(jnp.int32, (length, blocks, width), 0)
    k = lax.broadcasted_iota(jnp.int32, (length, blocks, width), 1) * (length // blocks)
    k = k + start + lax.broadcasted_iota(jnp.int32, (length, blocks, width), 2)
    phases = w * k % length
    angles = phases.astype(jnp.float32) * (2.0 * math.pi / length)
    factor = 1.0 / math.sqrt(length)
    return jnp.stack([jnp.cos(angles) * factor, -jnp.sin(angles) * factor], axis=1).astype(jnp.bfloat16)


def interleaved(index):
    return index // 2, index % 2


def blocked(kb):
    def split(index):
        blk, rest = index // (2 * kb), index % (2 * kb)
        return blk * kb + rest % kb, rest // kb

    return split


CHUNKS = 2


def on_device(features, filters, anchors):
    frames = lax.psum(1, "gop")
    blocks = lax.psum(1, "row")
    _, hb, columns, chans = features.shape
    height = filters.shape[1]
    wb = columns // blocks
    kb = height // frames
    part = wb // CHUNKS
    lanes = part * chans
    me = lax.axis_index("gop")

    shifts = [[(i, (i + s) % frames) for i in range(frames)] for s in range(frames)]

    x = features[0]
    gains = lax.dynamic_slice_in_dim(filters, me * kb, kb, axis=1)
    gains = gains.transpose(0, 2, 1, 3, 4)

    def mix(every, gain):
        outs = []
        for s in range(frames):
            frame = (me + s) % frames
            picks = (
                (me - frame) % frames,
                (me - anchors[frame, 0]) % frames,
                (me - anchors[frame, 1]) % frames,
            )
            sources = [lax.dynamic_index_in_dim(every, pick, 0, keepdims=False) for pick in picks]
            real_part = jnp.zeros((kb, lanes), jnp.float32)
            imag_part = jnp.zeros((kb, lanes), jnp.float32)
            for which_one in range(3):
                source_real = sources[which_one][0].astype(jnp.float32)
                source_imag = sources[which_one][1].astype(jnp.float32)
                gain_real = gain[which_one, 0]
                gain_imag = gain[which_one, 1]
                real_part = real_part + gain_real * source_real - gain_imag * source_imag
                imag_part = imag_part + gain_real * source_imag + gain_imag * source_real
            outs.append(jnp.stack([real_part, imag_part]).astype(jnp.bfloat16))
        return outs

    def exchange(pieces):
        return [pieces[0]] + [lax.ppermute(pieces[s], "gop", shifts[s]) for s in range(1, frames)]

    chunks = [slice(c * part, (c + 1) * part) for c in range(CHUNKS)]
    pieces = [row_piece(columns, blocks, c * part, part) for c in range(CHUNKS)]

    def row_transform(chunk):
        return jnp.einsum(
            "hwc,wprk->rhpkc", x, pieces[chunk], preferred_element_type=jnp.float32
        ).astype(jnp.bfloat16)

    def column_transform(slab):
        spectra = jnp.dot(
            forward_cols, slab.reshape(2 * height, lanes), preferred_element_type=jnp.float32
        ).astype(jnp.bfloat16)
        return spectra.reshape(frames, 2, kb, lanes)

    rowwise = row_transform(0)
    after = rowwise[0, 0, 0, 0, 0].astype(jnp.float32)
    slabs = [lax.all_to_all(rowwise, "row", 0, 0, tiled=True)]
    natural = column_matrix(height, -1.0, blocked(kb), interleaved, after).reshape(frames, 2 * kb, 2 * height)
    order = lax.broadcasted_iota(jnp.int32, (frames,), 0)
    forward_cols = jnp.take(natural, (me + order) % frames, axis=0).reshape(2 * height, 2 * height)
    inverse_cols = jnp.take(natural, (me - order) % frames, axis=0).reshape(2 * height, 2 * height).T
    forward_cols, inverse_cols = lax.optimization_barrier((forward_cols, inverse_cols))
    everys = []
    for chunk in range(CHUNKS):
        spectra = column_transform(slabs[chunk])
        if chunk + 1 < CHUNKS:
            ahead = row_transform(chunk + 1)
            rowwise = ahead
            slabs.append(lax.all_to_all(rowwise, "row", 0, 0, tiled=True))
        if chunk:
            spectra, _ = lax.optimization_barrier((spectra, everys[-1]))
        everys.append(jnp.stack(exchange([spectra[s] for s in range(frames)])))
    mines = []
    for chunk in range(CHUNKS):
        gain = gains[:, :, :, chunks[chunk]].reshape(3, 2, kb, lanes).astype(jnp.float32)
        outs = mix(everys[chunk], gain)
        if chunk:
            outs, _ = lax.optimization_barrier((outs, mines[-1]))
        mines.append(jnp.stack(exchange(outs)))
    total = x.astype(jnp.float32)
    for chunk in range(CHUNKS):
        back = jnp.dot(
            inverse_cols, mines[chunk].reshape(2 * height, lanes), preferred_element_type=jnp.float32
        ).astype(jnp.bfloat16)
        back = back.reshape(blocks, 2 * hb, lanes)
        rows_back = lax.all_to_all(back, "row", 0, 0, tiled=True)
        rows_back = rows_back.reshape(blocks, hb, 2, part, chans)
        total = total + jnp.einsum(
            "rhpkc,wprk->hwc", rows_back, pieces[chunk], preferred_element_type=jnp.float32
        )
    return total.astype(jnp.bfloat16)[None]


def solution(mesh):
    in_specs = (P("gop", "row", None, None), P(None, None, None, "row", None), P())
    out_specs = P("gop", "row", None, None)

    return jax.shard_map(on_device, mesh=mesh, in_specs=in_specs, out_specs=out_specs, check_vma=False)
```
